512 devices in a mesh: replica: 8 (over x, core), shard: 8 (over z), tensor: 8 (over y).
Axes of the slice: x: 4, y: 8, z: 8, core: 2. Of those that a mesh axis runs over, the one named last changes fastest.
Arguments:
- inproj_grads: bfloat16 [8, 1536, 3328], P('replica', 'shard', 'tensor'), may hold values from -6 to 6
- inproj_error: float32 [8, 1536, 3328], P('replica', 'shard', 'tensor'), may hold values from -6 to 6
- inproj_weight: float32 [1536, 3328], P('shard', 'tensor'), may hold values from -6 to 6
- inproj_moment: float32 [1536, 3328], P('shard', 'tensor'), may hold values from -6 to 6
- inproj_query: float32 [3328, 32], P('tensor'), may hold values from -0.109375 to 0.109375
- outproj_grads: bfloat16 [8, 3072, 1536], P('replica', 'shard', 'tensor'), may hold values from -6 to 6
- outproj_error: float32 [8, 3072, 1536], P('replica', 'shard', 'tensor'), may hold values from -6 to 6
- outproj_weight: float32 [3072, 1536], P('shard', 'tensor'), may hold values from -6 to 6
- outproj_moment: float32 [3072, 1536], P('shard', 'tensor'), may hold values from -6 to 6
- outproj_query: float32 [1536, 32], P('tensor'), may hold values from -0.15625 to 0.15625
Outputs:
- inproj_master: float32 [1536, 3328], P('shard', 'tensor')
- inproj_velocity: float32 [1536, 3328], P('shard', 'tensor')
- inproj_residue: float32 [8, 1536, 3328], P('replica', 'shard', 'tensor')
- inproj_basis: float32 [3328, 32], P('tensor')
- outproj_master: float32 [3072, 1536], P('shard', 'tensor')
- outproj_velocity: float32 [3072, 1536], P('shard', 'tensor')
- outproj_residue: float32 [8, 3072, 1536], P('replica', 'shard', 'tensor')
- outproj_basis: float32 [1536, 32], P('tensor')
The draws below stay inside these ranges and needn't reach their ends.
All inputs are finite; a program needn't handle non-finite values.
Results may differ from the reference program's by a relative error of at most 0.0003.
Values sent between devices are 32-bit elements; how exact they have to be, the bound alone decides.
No kernel may reach another device: no remote copies, remote signals or barrier semaphores. Data moves between devices by JAX's collectives and lax.ppermute only.
A program may use at most 64 MiB of HBM per device.

```python
import jax
import jax.numpy as jnp
from jax import lax

D = 1536
D_INNER = 3072
RANK = 32
ROUNDS = 2
NS_STEPS = 4
XBC = 3328
N_REPLICA = 8


def shard_levels(rng, shape, pieces, low, high):
    factor_of = 1.0
    for position, shards_of in pieces:
        heights = jax.random.uniform(jax.random.fold_in(jax.random.fold_in(rng, 6), position), (shards_of,), jnp.float32, low / len(pieces), high / len(pieces))
        factor_of = factor_of * jnp.repeat(jnp.exp(heights), shape[position] // shards_of).reshape((-1,) + (1,) * (len(shape) - 1 - position))
    return factor_of


def noise(stream_key, dims, width, limit, shards=(), kind=jnp.bfloat16):
    loudness = shard_levels(stream_key, dims, shards, -0.22, 0.18) if shards else 1.0
    values = jax.random.normal(stream_key, dims, jnp.float32) * width * loudness
    return jnp.minimum(jnp.maximum(values, -limit), limit).astype(kind)


def setup_inputs(seed: int = 0) -> dict:
    splits = jax.random.split(jax.random.key(seed), 11)
    inproj_grads = noise(splits[0], (N_REPLICA, D, XBC), 1.0, 6.0, ((0, 8), (1, 8), (2, 8)))
    inproj_error = noise(splits[1], (N_REPLICA, D, XBC), 0.5, 6.0, ((0, 8), (1, 8), (2, 8)), jnp.float32)
    inproj_weight = noise(splits[2], (D, XBC), 0.5, 6.0, ((0, 8), (1, 8)), jnp.float32)
    inproj_moment = noise(splits[3], (D, XBC), 0.5, 6.0, ((0, 8), (1, 8)), jnp.float32)
    inproj_query = noise(splits[4], (XBC, RANK), XBC ** -0.5, 0.109375, ((0, 8),), jnp.float32)
    outproj_grads = noise(splits[5], (N_REPLICA, D_INNER, D), 1.0, 6.0, ((0, 8), (1, 8), (2, 8)))
    outproj_error = noise(splits[6], (N_REPLICA, D_INNER, D), 0.5, 6.0, ((0, 8), (1, 8), (2, 8)), jnp.float32)
    outproj_weight = noise(splits[7], (D_INNER, D), 0.5, 6.0, ((0, 8), (1, 8)), jnp.float32)
    outproj_moment = noise(splits[8], (D_INNER, D), 0.5, 6.0, ((0, 8), (1, 8)), jnp.float32)
    outproj_query = noise(splits[9], (D, RANK), D ** -0.5, 0.15625, ((0, 8),), jnp.float32)
    return dict(inproj_grads=inproj_grads, inproj_error=inproj_error, inproj_weight=inproj_weight, inproj_moment=inproj_moment, inproj_query=inproj_query, outproj_grads=outproj_grads, outproj_error=outproj_error, outproj_weight=outproj_weight, outproj_moment=outproj_moment, outproj_query=outproj_query)


MOMENTUM_DECAY = 0.9
LEARN_RATE = 0.1
EPSILON = 1e-06

def precise_dot(left, right):
    return jnp.dot(left, right, precision=lax.Precision.HIGHEST, preferred_element_type=jnp.float32)

def inverse_root(gram_sum):
    identity = jnp.eye(gram_sum.shape[0], dtype=jnp.float32)
    norm_scale = jnp.sqrt(jnp.sum(gram_sum * gram_sum) + EPSILON)
    current = gram_sum / norm_scale
    inverse = identity
    for sweep in range(NS_STEPS):
        middle = 0.5 * (3.0 * identity - precise_dot(inverse, current))
        current = precise_dot(current, middle)
        inverse = precise_dot(middle, inverse)
    return inverse / jnp.sqrt(norm_scale)

def compress(grads, error, weight, moment, query):
    merged = grads.astype(jnp.float32) + error
    for power_round in range(ROUNDS):
        projected = jnp.einsum('rnm,mk->nk', merged, query, precision=lax.Precision.HIGHEST) / N_REPLICA
        gram_sum = precise_dot(projected.T, projected)
        orthonormal = precise_dot(projected, inverse_root(gram_sum))
        query = jnp.einsum('rnm,nk->mk', merged, orthonormal, precision=lax.Precision.HIGHEST) / N_REPLICA
    approx = precise_dot(orthonormal, query.T)
    residue = merged - approx[None]
    velocity = MOMENTUM_DECAY * moment + approx
    master = weight - LEARN_RATE * velocity
    return (master, velocity, residue, query)

def reference(inproj_grads, inproj_error, inproj_weight, inproj_moment, inproj_query, outproj_grads, outproj_error, outproj_weight, outproj_moment, outproj_query):
    first = compress(inproj_grads, inproj_error, inproj_weight, inproj_moment, inproj_query)
    second = compress(outproj_grads, outproj_error, outproj_weight, outproj_moment, outproj_query)
    return (first[0], first[1], first[2], first[3], second[0], second[1], second[2], second[3])
```

```python
import jax
import jax.numpy as jnp
from jax import lax
from jax.sharding import PartitionSpec as P

ROUNDS = 2
NS_STEPS = 4


MOMENTUM_DECAY = 0.9
LEARN_RATE = 0.1
EPSILON = 1e-06


def precise_dot(left, right):
    return jnp.dot(left, right, precision=lax.Precision.HIGHEST, preferred_element_type=jnp.float32)


def inverse_root(gram_sum):
    identity = jnp.eye(gram_sum.shape[0], dtype=jnp.float32)
    norm_scale = jnp.sqrt(jnp.sum(gram_sum * gram_sum) + EPSILON)
    current = gram_sum / norm_scale
    inverse = identity
    for sweep in range(NS_STEPS):
        middle = 0.5 * (3.0 * identity - precise_dot(inverse, current))
        current = precise_dot(current, middle)
        inverse = precise_dot(middle, inverse)
    return inverse / jnp.sqrt(norm_scale)


def gather_sum(x, axis):
    n = lax.axis_size(axis)
    copies = lax.all_to_all(jnp.broadcast_to(x[None], (n,) + x.shape), axis, 0, 0, tiled=False)
    return jnp.sum(copies, axis=0)


def all_sum(x, axes):
    for axis in axes:
        x = gather_sum(x, axis)
    return x


def finish(merged, orthonormal, query, weight, moment):
    approx = precise_dot(orthonormal, query.T)
    residue = (merged - approx)[None]
    velocity = MOMENTUM_DECAY * moment + approx
    master = weight - LEARN_RATE * velocity
    return (master, velocity, residue, query)


def per_device(
    inproj_grads,
    inproj_error,
    inproj_weight,
    inproj_moment,
    inproj_query,
    outproj_grads,
    outproj_error,
    outproj_weight,
    outproj_moment,
    outproj_query,
):
    replicas = lax.axis_size("replica")
    first_replica = (lax.axis_index("replica") == 0).astype(jnp.float32)
    merged = (
        inproj_grads[0].astype(jnp.float32) + inproj_error[0],
        outproj_grads[0].astype(jnp.float32) + outproj_error[0],
    )
    rows = [m.shape[0] for m in merged]
    cols = [m.shape[1] for m in merged]
    queries = [inproj_query, outproj_query]
    for power_round in range(ROUNDS):
        partial = jnp.concatenate([precise_dot(m, q) for m, q in zip(merged, queries)], axis=0)
        summed = all_sum(partial, ("replica", "tensor")) / replicas
        projected = [summed[: rows[0]], summed[rows[0] :]]
        pieces = []
        for m, p in zip(merged, projected):
            pieces.append(
                jnp.einsum(
                    "nm,nk->mk",
                    m,
                    p,
                    precision=lax.Precision.HIGHEST,
                    preferred_element_type=jnp.float32,
                )
            )
        for p in projected:
            pieces.append(precise_dot(p.T, p) * first_replica)
        column = all_sum(jnp.concatenate(pieces, axis=0), ("replica", "shard"))
        offsets = [0, cols[0], cols[0] + cols[1]]
        grams = [column[offsets[2] : offsets[2] + 32], column[offsets[2] + 32 : offsets[2] + 64]]
        inverses = [inverse_root(g) for g in grams]
        orthos = [precise_dot(p, z) for p, z in zip(projected, inverses)]
        queries = [
            precise_dot(column[offsets[i] : offsets[i + 1]], inverses[i]) / replicas for i in range(2)
        ]
    first = finish(merged[0], orthos[0], queries[0], inproj_weight, inproj_moment)
    second = finish(merged[1], orthos[1], queries[1], outproj_weight, outproj_moment)
    return (first[0], first[1], first[2], first[3], second[0], second[1], second[2], second[3])


def solution(mesh):
    return jax.shard_map(
        per_device,
        mesh=mesh,
        in_specs=(
            P("replica", "shard", "tensor"),
            P("replica", "shard", "tensor"),
            P("shard", "tensor"),
            P("shard", "tensor"),
            P("tensor", None),
            P("replica", "shard", "tensor"),
            P("replica", "shard", "tensor"),
            P("shard", "tensor"),
            P("shard", "tensor"),
            P("tensor", None),
        ),
        out_specs=(
            P("shard", "tensor"),
            P("shard", "tensor"),
            P("replica", "shard", "tensor"),
            P("tensor", None),
            P("shard", "tensor"),
            P("shard", "tensor"),
            P("replica", "shard", "tensor"),
            P("tensor", None),
        ),
        check_vma=False,
    )
```

```python
import jax
import jax.numpy as jnp
from jax import lax
from jax.sharding import PartitionSpec as P

ROUNDS = 2
NS_STEPS = 4


MOMENTUM_DECAY = 0.9
LEARN_RATE = 0.1
EPSILON = 1e-06


def precise_dot(left, right):
    return jnp.dot(left, right, precision=lax.Precision.HIGHEST, preferred_element_type=jnp.float32)


def inverse_root(gram_sum):
    identity = jnp.eye(gram_sum.shape[0], dtype=jnp.float32)
    norm_scale = jnp.sqrt(jnp.sum(gram_sum * gram_sum) + EPSILON)
    current = gram_sum / norm_scale
    inverse = identity
    for sweep in range(NS_STEPS):
        middle = 0.5 * (3.0 * identity - precise_dot(inverse, current))
        current = precise_dot(current, middle)
        inverse = precise_dot(middle, inverse)
    return inverse / jnp.sqrt(norm_scale)


def gather_sum(x, axis):
    n = lax.axis_size(axis)
    copies = lax.all_to_all(jnp.broadcast_to(x[None], (n,) + x.shape), axis, 0, 0, tiled=False)
    return jnp.sum(copies, axis=0)


def all_sum(x, axes):
    for axis in axes:
        x = gather_sum(x, axis)
    return x


def finish(merged, orthonormal, query, weight, moment):
    approx = precise_dot(orthonormal, query.T)
    residue = (merged - approx)[None]
    velocity = MOMENTUM_DECAY * moment + approx
    master = weight - LEARN_RATE * velocity
    return (master, velocity, residue, query)


def replica_total(blocks):
    n = lax.axis_size("replica")
    d = 1
    while d < n:
        pairs = [(i, i ^ d) for i in range(n)]
        moved = lax.ppermute(blocks, "replica", pairs)
        blocks = tuple(b + m for b, m in zip(blocks, moved))
        d *= 2
    return blocks


def contract_rows(m, p):
    return jnp.einsum(
        "nm,nk->mk",
        m,
        p,
        precision=lax.Precision.HIGHEST,
        preferred_element_type=jnp.float32,
    )


def per_device(
    inproj_grads,
    inproj_error,
    inproj_weight,
    inproj_moment,
    inproj_query,
    outproj_grads,
    outproj_error,
    outproj_weight,
    outproj_moment,
    outproj_query,
):
    replicas = lax.axis_size("replica")
    first_replica = (lax.axis_index("replica") == 0).astype(jnp.float32)
    merged = (
        inproj_grads[0].astype(jnp.float32) + inproj_error[0],
        outproj_grads[0].astype(jnp.float32) + outproj_error[0],
    )
    total = replica_total(merged)
    rows = [m.shape[0] for m in merged]
    cols = [m.shape[1] for m in merged]
    rank = inproj_query.shape[1]
    queries = [inproj_query, outproj_query]
    for power_round in range(ROUNDS):
        if power_round == 0:
            source, row_axes, col_axes, gram_weight = merged, ("replica", "tensor"), ("replica", "shard"), first_replica
        else:
            source, row_axes, col_axes, gram_weight = total, ("tensor",), ("shard",), 1.0
        partial = jnp.concatenate([precise_dot(m, q) for m, q in zip(source, queries)], axis=0)
        summed = all_sum(partial, row_axes) / replicas
        projected = [summed[: rows[0]], summed[rows[0] :]]
        pieces = [contract_rows(m, p) for m, p in zip(source, projected)]
        pieces += [precise_dot(p.T, p) * gram_weight for p in projected]
        column = all_sum(jnp.concatenate(pieces, axis=0), col_axes)
        offsets = [0, cols[0], cols[0] + cols[1]]
        grams = [column[offsets[2] : offsets[2] + rank], column[offsets[2] + rank : offsets[2] + 2 * rank]]
        inverses = [inverse_root(g) for g in grams]
        orthos = [precise_dot(p, z) for p, z in zip(projected, inverses)]
        queries = [
            precise_dot(column[offsets[i] : offsets[i + 1]], inverses[i]) / replicas for i in range(2)
        ]
    first = finish(merged[0], orthos[0], queries[0], inproj_weight, inproj_moment)
    second = finish(merged[1], orthos[1], queries[1], outproj_weight, outproj_moment)
    return (first[0], first[1], first[2], first[3], second[0], second[1], second[2], second[3])


def solution(mesh):
    return jax.shard_map(
        per_device,
        mesh=mesh,
        in_specs=(
            P("replica", "shard", "tensor"),
            P("replica", "shard", "tensor"),
            P("shard", "tensor"),
            P("shard", "tensor"),
            P("tensor", None),
            P("replica", "shard", "tensor"),
            P("replica", "shard", "tensor"),
            P("shard", "tensor"),
            P("shard", "tensor"),
            P("tensor", None),
        ),
        out_specs=(
            P("shard", "tensor"),
            P("shard", "tensor"),
            P("replica", "shard", "tensor"),
            P("tensor", None),
            P("shard", "tensor"),
            P("shard", "tensor"),
            P("replica", "shard", "tensor"),
            P("tensor", None),
        ),
        check_vma=False,
    )
```

```python
import jax
import jax.numpy as jnp
from jax import lax
from jax.sharding import PartitionSpec as P


ROUNDS = 2
NS_STEPS = 4


MOMENTUM_DECAY = 0.9
LEARN_RATE = 0.1
EPSILON = 1e-06


def precise_dot(left, right):
    return jnp.dot(left, right, precision=lax.Precision.HIGHEST, preferred_element_type=jnp.float32)


def batched_dot(left, right):
    return jnp.einsum(
        "bij,bjk->bik",
        left,
        right,
        precision=lax.Precision.HIGHEST,
        preferred_element_type=jnp.float32,
    )


def inverse_root(gram_sum):
    identity = jnp.eye(gram_sum.shape[-1], dtype=jnp.float32)[None]
    norm_scale = jnp.sqrt(jnp.sum(gram_sum * gram_sum, axis=(1, 2), keepdims=True) + EPSILON)
    current = gram_sum / norm_scale
    inverse = jnp.broadcast_to(identity, gram_sum.shape)
    for _ in range(NS_STEPS):
        middle = 0.5 * (3.0 * identity - batched_dot(inverse, current))
        current = batched_dot(current, middle)
        inverse = batched_dot(middle, inverse)
    return inverse / jnp.sqrt(norm_scale)


def gather_sum(x, axis):
    n = lax.axis_size(axis)
    copies = lax.all_to_all(jnp.broadcast_to(x[None], (n,) + x.shape), axis, 0, 0, tiled=False)
    return jnp.sum(copies, axis=0)


def all_sum(x, axes):
    for axis in axes:
        x = gather_sum(x, axis)
    return x


def finish(merged, orthonormal, query, weight, moment):
    approx = precise_dot(orthonormal, query.T)
    residue = (merged - approx)[None]
    velocity = MOMENTUM_DECAY * moment + approx
    master = weight - LEARN_RATE * velocity
    return (master, velocity, residue, query)


def replica_total(blocks, order):
    n = lax.axis_size("replica")
    height = blocks[0].shape[0]
    flat = jnp.concatenate([b.reshape(height, -1) for b in blocks], axis=1)
    for d in order:
        pairs = [(i, i ^ d) for i in range(n)]
        moved = lax.ppermute(flat, "replica", pairs)
        flat = flat + moved
    widths = [b.size // height for b in blocks]
    first = flat[:, : widths[0]].reshape(blocks[0].shape)
    second = flat[:, widths[0] :].reshape(blocks[1].shape)
    return (first, second)


def contract_rows(m, p):
    return jnp.einsum(
        "nm,nk->mk",
        m,
        p,
        precision=lax.Precision.HIGHEST,
        preferred_element_type=jnp.float32,
    )


def per_device(
    inproj_grads,
    inproj_error,
    inproj_weight,
    inproj_moment,
    inproj_query,
    outproj_grads,
    outproj_error,
    outproj_weight,
    outproj_moment,
    outproj_query,
):
    replicas = lax.axis_size("replica")
    merged = (
        inproj_grads[0].astype(jnp.float32) + inproj_error[0],
        outproj_grads[0].astype(jnp.float32) + outproj_error[0],
    )
    total = replica_total(merged, (2, 4, 1))
    rows = [m.shape[0] for m in merged]
    cols = [m.shape[1] for m in merged]
    rank = inproj_query.shape[1]
    queries = [inproj_query, outproj_query]
    for power_round in range(ROUNDS):
        if power_round == 0:
            rows_source, row_axes = merged, ("replica", "tensor")
        else:
            rows_source, row_axes = total, ("tensor",)
        partial = jnp.concatenate([precise_dot(m, q) for m, q in zip(rows_source, queries)], axis=0)
        summed = all_sum(partial, row_axes) / replicas
        projected = [summed[: rows[0]], summed[rows[0] :]]
        pieces = [contract_rows(m, p) for m, p in zip(total, projected)]
        pieces += [precise_dot(p.T, p) for p in projected]
        column = all_sum(jnp.concatenate(pieces, axis=0), ("shard",))
        offsets = [0, cols[0], cols[0] + cols[1]]
        grams = column[offsets[2] :].reshape(2, rank, rank)
        inverses = inverse_root(grams)
        orthos = [precise_dot(p, inverses[i]) for i, p in enumerate(projected)]
        queries = [
            precise_dot(column[offsets[i] : offsets[i + 1]], inverses[i]) / replicas for i in range(2)
        ]
    first = finish(merged[0], orthos[0], queries[0], inproj_weight, inproj_moment)
    second = finish(merged[1], orthos[1], queries[1], outproj_weight, outproj_moment)
    return (first[0], first[1], first[2], first[3], second[0], second[1], second[2], second[3])


def solution(mesh):
    return jax.shard_map(
        per_device,
        mesh=mesh,
        in_specs=(
            P("replica", "shard", "tensor"),
            P("replica", "shard", "tensor"),
            P("shard", "tensor"),
            P("shard", "tensor"),
            P("tensor", None),
            P("replica", "shard", "tensor"),
            P("replica", "shard", "tensor"),
            P("shard", "tensor"),
            P("shard", "tensor"),
            P("tensor", None),
        ),
        out_specs=(
            P("shard", "tensor"),
            P("shard", "tensor"),
            P("replica", "shard", "tensor"),
            P("tensor", None),
            P("shard", "tensor"),
            P("shard", "tensor"),
            P("replica", "shard", "tensor"),
            P("tensor", None),
        ),
        check_vma=False,
    )
```

```python
import jax
import jax.numpy as jnp
from jax import lax
from jax.sharding import PartitionSpec as P


ROUNDS = 2
NS_STEPS = 4


MOMENTUM_DECAY = 0.9
LEARN_RATE = 0.1
EPSILON = 1e-06


def precise_dot(left, right):
    return jnp.dot(left, right, precision=lax.Precision.HIGHEST, preferred_element_type=jnp.float32)


def batched_dot(left, right):
    return jnp.einsum(
        "bij,bjk->bik",
        left,
        right,
        precision=lax.Precision.HIGHEST,
        preferred_element_type=jnp.float32,
    )


def inverse_root(gram_sum):
    identity = jnp.eye(gram_sum.shape[-1], dtype=jnp.float32)[None]
    norm_scale = jnp.sqrt(jnp.sum(gram_sum * gram_sum, axis=(1, 2), keepdims=True) + EPSILON)
    current = gram_sum / norm_scale
    inverse = jnp.broadcast_to(identity, gram_sum.shape)
    for _ in range(NS_STEPS):
        middle = 0.5 * (3.0 * identity - batched_dot(inverse, current))
        current = batched_dot(current, middle)
        inverse = batched_dot(middle, inverse)
    return inverse / jnp.sqrt(norm_scale)


def gather_sum(x, axis):
    n = lax.axis_size(axis)
    copies = lax.all_to_all(jnp.broadcast_to(x[None], (n,) + x.shape), axis, 0, 0, tiled=False)
    return jnp.sum(copies, axis=0)


def finish(merged, orthonormal, query, weight, moment):
    approx = precise_dot(orthonormal, query.T)
    residue = (merged - approx)[None]
    velocity = MOMENTUM_DECAY * moment + approx
    master = weight - LEARN_RATE * velocity
    return (master, velocity, residue, query)


def replica_total(blocks, order):
    n = lax.axis_size("replica")
    height = blocks[0].shape[0]
    flat = jnp.concatenate([b.reshape(height, -1) for b in blocks], axis=1)
    for d in order:
        pairs = [(i, i ^ d) for i in range(n)]
        moved = lax.ppermute(flat, "replica", pairs)
        flat = flat + moved
    widths = [b.size // height for b in blocks]
    first = flat[:, : widths[0]].reshape(blocks[0].shape)
    second = flat[:, widths[0] :].reshape(blocks[1].shape)
    return (first, second)


def contract_rows(m, p):
    return jnp.einsum(
        "nm,nk->mk",
        m,
        p,
        precision=lax.Precision.HIGHEST,
        preferred_element_type=jnp.float32,
    )


def pad_rows(x, height):
    return jnp.pad(x, ((0, height - x.shape[0]), (0, 0)))


def per_device(
    inproj_grads,
    inproj_error,
    inproj_weight,
    inproj_moment,
    inproj_query,
    outproj_grads,
    outproj_error,
    outproj_weight,
    outproj_moment,
    outproj_query,
):
    replicas = lax.axis_size("replica")
    merged = (
        inproj_grads[0].astype(jnp.float32) + inproj_error[0],
        outproj_grads[0].astype(jnp.float32) + outproj_error[0],
    )
    total = replica_total(merged, (2, 4, 1))
    rows = [m.shape[0] for m in merged]
    cols = [m.shape[1] for m in merged]
    rank = inproj_query.shape[1]
    first_core = lax.axis_index("replica") % 2 == 0

    def pick(for_inproj, for_outproj):
        return jnp.where(first_core, for_inproj, for_outproj)

    row_pad = max(rows)
    col_pad = max(cols) + rank

    def column_step(projected):
        p_in, p_out = projected[: rows[0]], projected[: rows[1]]
        side_in = jnp.concatenate([contract_rows(total[0], p_in), precise_dot(p_in.T, p_in)], axis=0)
        side_out = jnp.concatenate([contract_rows(total[1], p_out), precise_dot(p_out.T, p_out)], axis=0)
        mine = pick(pad_rows(side_in, col_pad), pad_rows(side_out, col_pad))
        column = gather_sum(mine, "shard")
        gram = pick(column[cols[0] : cols[0] + rank], column[cols[1] : cols[1] + rank])
        inverse = inverse_root(gram[None])[0]
        return precise_dot(projected, inverse), precise_dot(column, inverse) / replicas

    partial = jnp.concatenate([precise_dot(m, q) for m, q in zip(merged, (inproj_query, outproj_query))], axis=0)
    summed = gather_sum(partial, "replica")
    mine = pick(pad_rows(summed[: rows[0]], row_pad), pad_rows(summed[rows[0] :], row_pad))
    projected = gather_sum(mine, "tensor") / replicas
    ortho, query = column_step(projected)
    for _ in range(1, ROUNDS):
        part_in = precise_dot(total[0], query[: cols[0]])
        part_out = precise_dot(total[1], query[: cols[1]])
        mine = pick(pad_rows(part_in, row_pad), pad_rows(part_out, row_pad))
        projected = gather_sum(mine, "tensor") / replicas
        ortho, query = column_step(projected)
    held = jnp.concatenate([ortho, query], axis=0)
    n = lax.axis_size("replica")
    other = lax.ppermute(held, "replica", [(i, i ^ 1) for i in range(n)])
    own_in = pick(held, other)
    own_out = pick(other, held)
    orthos = [own_in[: rows[0]], own_out[: rows[1]]]
    queries = [own_in[row_pad : row_pad + cols[0]], own_out[row_pad : row_pad + cols[1]]]
    first = finish(merged[0], orthos[0], queries[0], inproj_weight, inproj_moment)
    second = finish(merged[1], orthos[1], queries[1], outproj_weight, outproj_moment)
    return (first[0], first[1], first[2], first[3], second[0], second[1], second[2], second[3])


def solution(mesh):
    return jax.shard_map(
        per_device,
        mesh=mesh,
        in_specs=(
            P("replica", "shard", "tensor"),
            P("replica", "shard", "tensor"),
            P("shard", "tensor"),
            P("shard", "tensor"),
            P("tensor", None),
            P("replica", "shard", "tensor"),
            P("replica", "shard", "tensor"),
            P("shard", "tensor"),
            P("shard", "tensor"),
            P("tensor", None),
        ),
        out_specs=(
            P("shard", "tensor"),
            P("shard", "tensor"),
            P("replica", "shard", "tensor"),
            P("tensor", None),
            P("shard", "tensor"),
            P("shard", "tensor"),
            P("replica", "shard", "tensor"),
            P("tensor", None),
        ),
        check_vma=False,
    )
```

```python
import jax
import jax.numpy as jnp
from jax import lax
from jax.sharding import PartitionSpec as P


ROUNDS = 2
NS_STEPS = 4


MOMENTUM_DECAY = 0.9
LEARN_RATE = 0.1
EPSILON = 1e-06


def precise_dot(left, right):
    return jnp.dot(left, right, precision=lax.Precision.HIGHEST, preferred_element_type=jnp.float32)


def batched_dot(left, right):
    return jnp.einsum(
        "bij,bjk->bik",
        left,
        right,
        precision=lax.Precision.HIGHEST,
        preferred_element_type=jnp.float32,
    )


def inverse_root(gram_sum):
    identity = jnp.eye(gram_sum.shape[-1], dtype=jnp.float32)[None]
    norm_scale = jnp.sqrt(jnp.sum(gram_sum * gram_sum, axis=(1, 2), keepdims=True) + EPSILON)
    current = gram_sum / norm_scale
    inverse = jnp.broadcast_to(identity, gram_sum.shape)
    for _ in range(NS_STEPS):
        middle = 0.5 * (3.0 * identity - batched_dot(inverse, current))
        current = batched_dot(current, middle)
        inverse = batched_dot(middle, inverse)
    return inverse / jnp.sqrt(norm_scale)


def gather_sum(x, axis):
    n = lax.axis_size(axis)
    copies = lax.all_to_all(jnp.broadcast_to(x[None], (n,) + x.shape), axis, 0, 0, tiled=False)
    return jnp.sum(copies, axis=0)


def finish(merged, orthonormal, query, weight, moment):
    approx = precise_dot(orthonormal, query.T)
    residue = (merged - approx)[None]
    velocity = MOMENTUM_DECAY * moment + approx
    master = weight - LEARN_RATE * velocity
    return (master, velocity, residue, query)


def replica_total(blocks, keep_first, order):
    n = lax.axis_size("replica")
    height, width = blocks[0].shape
    second = jnp.pad(blocks[1].reshape(height, -1), ((0, 0), (0, width - blocks[1].size // height)))
    held = jnp.where(keep_first, blocks[0], second)
    sent = jnp.where(keep_first, second, blocks[0])
    for d in order:
        pairs = [(i, i ^ d) for i in range(n)]
        moved = lax.ppermute(sent, "replica", pairs)
        held = held + moved
        sent = held
    return held, held[:, : blocks[1].size // height].reshape(blocks[1].shape)


def contract_rows(m, p):
    return jnp.einsum(
        "nm,nk->mk",
        m,
        p,
        precision=lax.Precision.HIGHEST,
        preferred_element_type=jnp.float32,
    )


def pad_rows(x, height):
    return jnp.pad(x, ((0, height - x.shape[0]), (0, 0)))


def per_device(
    inproj_grads,
    inproj_error,
    inproj_weight,
    inproj_moment,
    inproj_query,
    outproj_grads,
    outproj_error,
    outproj_weight,
    outproj_moment,
    outproj_query,
):
    replicas = lax.axis_size("replica")
    merged = (
        inproj_grads[0].astype(jnp.float32) + inproj_error[0],
        outproj_grads[0].astype(jnp.float32) + outproj_error[0],
    )
    rows = [m.shape[0] for m in merged]
    cols = [m.shape[1] for m in merged]
    rank = inproj_query.shape[1]
    first_core = lax.axis_index("replica") % 2 == 0
    total = replica_total(merged, first_core, (1, 2, 4))

    def pick(for_inproj, for_outproj):
        return jnp.where(first_core, for_inproj, for_outproj)

    row_pad = max(rows)
    col_pad = max(cols) + rank

    def column_step(projected):
        p_in, p_out = projected[: rows[0]], projected[: rows[1]]
        side_in = jnp.concatenate([contract_rows(total[0], p_in), precise_dot(p_in.T, p_in)], axis=0)
        side_out = jnp.concatenate([contract_rows(total[1], p_out), precise_dot(p_out.T, p_out)], axis=0)
        mine = pick(pad_rows(side_in, col_pad), pad_rows(side_out, col_pad))
        column = gather_sum(mine, "shard")
        gram = pick(column[cols[0] : cols[0] + rank], column[cols[1] : cols[1] + rank])
        inverse = inverse_root(gram[None])[0]
        return precise_dot(projected, inverse), precise_dot(column, inverse) / replicas

    partial = jnp.concatenate([precise_dot(m, q) for m, q in zip(merged, (inproj_query, outproj_query))], axis=0)
    summed = gather_sum(partial, "replica")
    mine = pick(pad_rows(summed[: rows[0]], row_pad), pad_rows(summed[rows[0] :], row_pad))
    projected = gather_sum(mine, "tensor") / replicas
    ortho, query = column_step(projected)
    for _ in range(1, ROUNDS):
        part_in = precise_dot(total[0], query[: cols[0]])
        part_out = precise_dot(total[1], query[: cols[1]])
        mine = pick(pad_rows(part_in, row_pad), pad_rows(part_out, row_pad))
        projected = gather_sum(mine, "tensor") / replicas
        ortho, query = column_step(projected)
    held = jnp.concatenate([ortho, query], axis=0)
    n = lax.axis_size("replica")
    other = lax.ppermute(held, "replica", [(i, i ^ 1) for i in range(n)])
    own_in = pick(held, other)
    own_out = pick(other, held)
    orthos = [own_in[: rows[0]], own_out[: rows[1]]]
    queries = [own_in[row_pad : row_pad + cols[0]], own_out[row_pad : row_pad + cols[1]]]
    first = finish(merged[0], orthos[0], queries[0], inproj_weight, inproj_moment)
    second = finish(merged[1], orthos[1], queries[1], outproj_weight, outproj_moment)
    return (first[0], first[1], first[2], first[3], second[0], second[1], second[2], second[3])


def solution(mesh):
    return jax.shard_map(
        per_device,
        mesh=mesh,
        in_specs=(
            P("replica", "shard", "tensor"),
            P("replica", "shard", "tensor"),
            P("shard", "tensor"),
            P("shard", "tensor"),
            P("tensor", None),
            P("replica", "shard", "tensor"),
            P("replica", "shard", "tensor"),
            P("shard", "tensor"),
            P("shard", "tensor"),
            P("tensor", None),
        ),
        out_specs=(
            P("shard", "tensor"),
            P("shard", "tensor"),
            P("replica", "shard", "tensor"),
            P("tensor", None),
            P("shard", "tensor"),
            P("shard", "tensor"),
            P("replica", "shard", "tensor"),
            P("tensor", None),
        ),
        check_vma=False,
    )
```

```python
import jax
import jax.numpy as jnp
from jax import lax
from jax.sharding import PartitionSpec as P


ROUNDS = 2
NS_STEPS = 4


MOMENTUM_DECAY = 0.9
LEARN_RATE = 0.1
EPSILON = 1e-06


def precise_dot(left, right):
    return jnp.dot(left, right, precision=lax.Precision.HIGHEST, preferred_element_type=jnp.float32)


def batched_dot(left, right):
    return jnp.einsum(
        "bij,bjk->bik",
        left,
        right,
        precision=lax.Precision.HIGHEST,
        preferred_element_type=jnp.float32,
    )


def inverse_root(gram_sum):
    identity = jnp.eye(gram_sum.shape[-1], dtype=jnp.float32)[None]
    norm_scale = jnp.sqrt(jnp.sum(gram_sum * gram_sum, axis=(1, 2), keepdims=True) + EPSILON)
    current = gram_sum / norm_scale
    inverse = jnp.broadcast_to(identity, gram_sum.shape)
    for _ in range(NS_STEPS):
        middle = 0.5 * (3.0 * identity - batched_dot(inverse, current))
        current = batched_dot(current, middle)
        inverse = batched_dot(middle, inverse)
    return inverse / jnp.sqrt(norm_scale)


def gather_sum(x, axis):
    n = lax.axis_size(axis)
    copies = lax.all_to_all(jnp.broadcast_to(x[None], (n,) + x.shape), axis, 0, 0, tiled=False)
    return jnp.sum(copies, axis=0)


def finish(merged, orthonormal, query, weight, moment):
    approx = precise_dot(orthonormal, query.T)
    residue = (merged - approx)[None]
    velocity = MOMENTUM_DECAY * moment + approx
    master = weight - LEARN_RATE * velocity
    return (master, velocity, residue, query)


def replica_total(blocks, keep_first, order):
    n = lax.axis_size("replica")
    height, width = blocks[0].shape
    second = jnp.pad(blocks[1].reshape(height, -1), ((0, 0), (0, width - blocks[1].size // height)))
    held = jnp.where(keep_first, blocks[0], second)
    sent = jnp.where(keep_first, second, blocks[0])
    for group in order:
        moved = [lax.ppermute(sent, "replica", [(i, i ^ d) for i in range(n)]) for d in group]
        if len(moved) == 1:
            held = held + moved[0]
        else:
            held = (held + moved[0]) + (moved[1] + moved[2])
        sent = held
    return held, held[:, : blocks[1].size // height].reshape(blocks[1].shape)


def contract_rows(m, p):
    return jnp.einsum(
        "nm,nk->mk",
        m,
        p,
        precision=lax.Precision.HIGHEST,
        preferred_element_type=jnp.float32,
    )


def pad_rows(x, height):
    return jnp.pad(x, ((0, height - x.shape[0]), (0, 0)))


def per_device(
    inproj_grads,
    inproj_error,
    inproj_weight,
    inproj_moment,
    inproj_query,
    outproj_grads,
    outproj_error,
    outproj_weight,
    outproj_moment,
    outproj_query,
):
    replicas = lax.axis_size("replica")
    merged = (
        inproj_grads[0].astype(jnp.float32) + inproj_error[0],
        outproj_grads[0].astype(jnp.float32) + outproj_error[0],
    )
    rows = [m.shape[0] for m in merged]
    cols = [m.shape[1] for m in merged]
    rank = inproj_query.shape[1]
    first_core = lax.axis_index("replica") % 2 == 0
    total = replica_total(merged, first_core, ((1,), (2, 4, 6)))

    def pick(for_inproj, for_outproj):
        return jnp.where(first_core, for_inproj, for_outproj)

    row_pad = max(rows)
    col_pad = max(cols) + rank

    def column_step(projected):
        p_in, p_out = projected[: rows[0]], projected[: rows[1]]
        side_in = jnp.concatenate([contract_rows(total[0], p_in), precise_dot(p_in.T, p_in)], axis=0)
        side_out = jnp.concatenate([contract_rows(total[1], p_out), precise_dot(p_out.T, p_out)], axis=0)
        mine = pick(pad_rows(side_in, col_pad), pad_rows(side_out, col_pad))
        column = gather_sum(mine, "shard")
        gram = pick(column[cols[0] : cols[0] + rank], column[cols[1] : cols[1] + rank])
        inverse = inverse_root(gram[None])[0]
        return precise_dot(projected, inverse), precise_dot(column, inverse) / replicas

    partial = jnp.concatenate([precise_dot(m, q) for m, q in zip(merged, (inproj_query, outproj_query))], axis=0)
    summed = gather_sum(partial, "replica")
    mine = pick(pad_rows(summed[: rows[0]], row_pad), pad_rows(summed[rows[0] :], row_pad))
    projected = gather_sum(mine, "tensor") / replicas
    ortho, query = column_step(projected)
    for _ in range(1, ROUNDS):
        part_in = precise_dot(total[0], query[: cols[0]])
        part_out = precise_dot(total[1], query[: cols[1]])
        mine = pick(pad_rows(part_in, row_pad), pad_rows(part_out, row_pad))
        projected = gather_sum(mine, "tensor") / replicas
        ortho, query = column_step(projected)
    held = jnp.concatenate([ortho, query], axis=0)
    n = lax.axis_size("replica")
    other = lax.ppermute(held, "replica", [(i, i ^ 1) for i in range(n)])
    own_in = pick(held, other)
    own_out = pick(other, held)
    orthos = [own_in[: rows[0]], own_out[: rows[1]]]
    queries = [own_in[row_pad : row_pad + cols[0]], own_out[row_pad : row_pad + cols[1]]]
    first = finish(merged[0], orthos[0], queries[0], inproj_weight, inproj_moment)
    second = finish(merged[1], orthos[1], queries[1], outproj_weight, outproj_moment)
    return (first[0], first[1], first[2], first[3], second[0], second[1], second[2], second[3])


def solution(mesh):
    return jax.shard_map(
        per_device,
        mesh=mesh,
        in_specs=(
            P("replica", "shard", "tensor"),
            P("replica", "shard", "tensor"),
            P("shard", "tensor"),
            P("shard", "tensor"),
            P("tensor", None),
            P("replica", "shard", "tensor"),
            P("replica", "shard", "tensor"),
            P("shard", "tensor"),
            P("shard", "tensor"),
            P("tensor", None),
        ),
        out_specs=(
            P("shard", "tensor"),
            P("shard", "tensor"),
            P("replica", "shard", "tensor"),
            P("tensor", None),
            P("shard", "tensor"),
            P("shard", "tensor"),
            P("replica", "shard", "tensor"),
            P("tensor", None),
        ),
        check_vma=False,
    )
```

```python
import jax
import jax.numpy as jnp
from jax import lax
from jax.experimental import pallas as pl
from jax.sharding import PartitionSpec as P


ROUNDS = 2
NS_STEPS = 4


MOMENTUM_DECAY = 0.9
LEARN_RATE = 0.1
EPSILON = 1e-06


def precise_dot(left, right):
    return jnp.dot(left, right, precision=lax.Precision.HIGHEST, preferred_element_type=jnp.float32)


def inverse_root_kernel(gram_ref, out_ref):
    gram = gram_ref[...]
    size = gram.shape[0]
    identity = (
        lax.broadcasted_iota(jnp.int32, (size, size), 0) == lax.broadcasted_iota(jnp.int32, (size, size), 1)
    ).astype(jnp.float32)
    squares = jnp.sum(jnp.sum(gram * gram, axis=1, keepdims=True), axis=0, keepdims=True)
    norm_scale = jnp.sqrt(squares + EPSILON)
    current = gram / norm_scale
    inverse = identity
    for _ in range(NS_STEPS):
        middle = 0.5 * (3.0 * identity - precise_dot(inverse, current))
        current = precise_dot(current, middle)
        inverse = precise_dot(middle, inverse)
    out_ref[...] = inverse / jnp.sqrt(norm_scale)


def inverse_root(gram_sum):
    return pl.pallas_call(
        inverse_root_kernel,
        out_shape=jax.ShapeDtypeStruct(gram_sum.shape, jnp.float32),
    )(gram_sum)


def gather_sum(x, axis):
    n = lax.axis_size(axis)
    copies = lax.all_to_all(jnp.broadcast_to(x[None], (n,) + x.shape), axis, 0, 0, tiled=False)
    return jnp.sum(copies, axis=0)


def finish(merged, orthonormal, query, weight, moment):
    approx = precise_dot(orthonormal, query.T)
    residue = (merged - approx)[None]
    velocity = MOMENTUM_DECAY * moment + approx
    master = weight - LEARN_RATE * velocity
    return (master, velocity, residue, query)


def replica_total(blocks, keep_first, order):
    n = lax.axis_size("replica")
    height, width = blocks[0].shape
    second = jnp.pad(blocks[1].reshape(height, -1), ((0, 0), (0, width - blocks[1].size // height)))
    held = jnp.where(keep_first, blocks[0], second)
    sent = jnp.where(keep_first, second, blocks[0])
    for d in order:
        pairs = [(i, i ^ d) for i in range(n)]
        moved = lax.ppermute(sent, "replica", pairs)
        held = held + moved
        sent = held
    return held, held[:, : blocks[1].size // height].reshape(blocks[1].shape)


def contract_rows(m, p):
    return jnp.einsum(
        "nm,nk->mk",
        m,
        p,
        precision=lax.Precision.HIGHEST,
        preferred_element_type=jnp.float32,
    )


def pad_rows(x, height):
    return jnp.pad(x, ((0, height - x.shape[0]), (0, 0)))


def per_device(
    inproj_grads,
    inproj_error,
    inproj_weight,
    inproj_moment,
    inproj_query,
    outproj_grads,
    outproj_error,
    outproj_weight,
    outproj_moment,
    outproj_query,
):
    replicas = lax.axis_size("replica")
    merged = (
        inproj_grads[0].astype(jnp.float32) + inproj_error[0],
        outproj_grads[0].astype(jnp.float32) + outproj_error[0],
    )
    rows = [m.shape[0] for m in merged]
    cols = [m.shape[1] for m in merged]
    rank = inproj_query.shape[1]
    first_core = lax.axis_index("replica") % 2 == 0
    total = replica_total(merged, first_core, (1, 2, 4))

    def pick(for_inproj, for_outproj):
        return jnp.where(first_core, for_inproj, for_outproj)

    row_pad = max(rows)
    col_pad = max(cols) + rank

    def column_step(projected):
        p_in, p_out = projected[: rows[0]], projected[: rows[1]]
        side_in = jnp.concatenate([contract_rows(total[0], p_in), precise_dot(p_in.T, p_in)], axis=0)
        side_out = jnp.concatenate([contract_rows(total[1], p_out), precise_dot(p_out.T, p_out)], axis=0)
        mine = pick(pad_rows(side_in, col_pad), pad_rows(side_out, col_pad))
        column = gather_sum(mine, "shard")
        gram = pick(column[cols[0] : cols[0] + rank], column[cols[1] : cols[1] + rank])
        inverse = inverse_root(gram)
        return precise_dot(projected, inverse), precise_dot(column, inverse) / replicas

    partial = jnp.concatenate([precise_dot(m, q) for m, q in zip(merged, (inproj_query, outproj_query))], axis=0)
    summed = gather_sum(partial, "replica")
    mine = pick(pad_rows(summed[: rows[0]], row_pad), pad_rows(summed[rows[0] :], row_pad))
    projected = gather_sum(mine, "tensor") / replicas
    ortho, query = column_step(projected)
    for _ in range(1, ROUNDS):
        part_in = precise_dot(total[0], query[: cols[0]])
        part_out = precise_dot(total[1], query[: cols[1]])
        mine = pick(pad_rows(part_in, row_pad), pad_rows(part_out, row_pad))
        projected = gather_sum(mine, "tensor") / replicas
        ortho, query = column_step(projected)
    held = jnp.concatenate([ortho, query], axis=0)
    n = lax.axis_size("replica")
    other = lax.ppermute(held, "replica", [(i, i ^ 1) for i in range(n)])
    own_in = pick(held, other)
    own_out = pick(other, held)
    orthos = [own_in[: rows[0]], own_out[: rows[1]]]
    queries = [own_in[row_pad : row_pad + cols[0]], own_out[row_pad : row_pad + cols[1]]]
    first = finish(merged[0], orthos[0], queries[0], inproj_weight, inproj_moment)
    second = finish(merged[1], orthos[1], queries[1], outproj_weight, outproj_moment)
    return (first[0], first[1], first[2], first[3], second[0], second[1], second[2], second[3])


def solution(mesh):
    return jax.shard_map(
        per_device,
        mesh=mesh,
        in_specs=(
            P("replica", "shard", "tensor"),
            P("replica", "shard", "tensor"),
            P("shard", "tensor"),
            P("shard", "tensor"),
            P("tensor", None),
            P("replica", "shard", "tensor"),
            P("replica", "shard", "tensor"),
            P("shard", "tensor"),
            P("shard", "tensor"),
            P("tensor", None),
        ),
        out_specs=(
            P("shard", "tensor"),
            P("shard", "tensor"),
            P("replica", "shard", "tensor"),
            P("tensor", None),
            P("shard", "tensor"),
            P("shard", "tensor"),
            P("replica", "shard", "tensor"),
            P("tensor", None),
        ),
        check_vma=False,
    )
```

```python
import jax
import jax.numpy as jnp
from jax import lax
from jax.sharding import PartitionSpec as P


ROUNDS = 2
NS_STEPS = 4


MOMENTUM_DECAY = 0.9
LEARN_RATE = 0.1
EPSILON = 1e-06


def precise_dot(left, right):
    return jnp.dot(left, right, precision=lax.Precision.HIGHEST, preferred_element_type=jnp.float32)


def batched_dot(left, right):
    return jnp.einsum(
        "bij,bjk->bik",
        left,
        right,
        precision=lax.Precision.HIGHEST,
        preferred_element_type=jnp.float32,
    )


def inverse_root(gram_sum):
    identity = jnp.eye(gram_sum.shape[-1], dtype=jnp.float32)[None]
    norm_scale = jnp.sqrt(jnp.sum(gram_sum * gram_sum, axis=(1, 2), keepdims=True) + EPSILON)
    current = gram_sum / norm_scale
    inverse = jnp.broadcast_to(identity, gram_sum.shape)
    for _ in range(NS_STEPS):
        middle = 0.5 * (3.0 * identity - batched_dot(inverse, current))
        current = batched_dot(current, middle)
        inverse = batched_dot(middle, inverse)
    return inverse / jnp.sqrt(norm_scale)


def gather_sum(x, axis):
    n = lax.axis_size(axis)
    copies = lax.all_to_all(jnp.broadcast_to(x[None], (n,) + x.shape), axis, 0, 0, tiled=False)
    return jnp.sum(copies, axis=0)


def finish(merged, orthonormal, query, weight, moment):
    approx = precise_dot(orthonormal, query.T)
    residue = (merged - approx)[None]
    velocity = MOMENTUM_DECAY * moment + approx
    master = weight - LEARN_RATE * velocity
    return (master, velocity, residue, query)


def replica_total(blocks, keep_first, order):
    n = lax.axis_size("replica")
    height, width = blocks[0].shape
    second = jnp.pad(blocks[1].reshape(height, -1), ((0, 0), (0, width - blocks[1].size // height)))
    held = jnp.where(keep_first, blocks[0], second)
    sent = jnp.where(keep_first, second, blocks[0])
    for d in order:
        pairs = [(i, i ^ d) for i in range(n)]
        moved = lax.ppermute(sent, "replica", pairs)
        held = held + moved
        sent = held
    return held, held[:, : blocks[1].size // height].reshape(blocks[1].shape)


def contract_rows(m, p):
    return jnp.einsum(
        "nm,nk->mk",
        m,
        p,
        precision=lax.Precision.HIGHEST,
        preferred_element_type=jnp.float32,
    )


def pad_rows(x, height):
    return jnp.pad(x, ((0, height - x.shape[0]), (0, 0)))


def per_device(
    inproj_grads,
    inproj_error,
    inproj_weight,
    inproj_moment,
    inproj_query,
    outproj_grads,
    outproj_error,
    outproj_weight,
    outproj_moment,
    outproj_query,
):
    replicas = lax.axis_size("replica")
    merged = (
        inproj_grads[0].astype(jnp.float32) + inproj_error[0],
        outproj_grads[0].astype(jnp.float32) + outproj_error[0],
    )
    rows = [m.shape[0] for m in merged]
    cols = [m.shape[1] for m in merged]
    rank = inproj_query.shape[1]
    first_core = lax.axis_index("replica") % 2 == 0
    total = replica_total(merged, first_core, (1, 2, 4))

    def pick(for_inproj, for_outproj):
        return jnp.where(first_core, for_inproj, for_outproj)

    row_pad = max(rows)
    col_pad = max(cols) + rank

    def column_step(projected):
        p_in, p_out = projected[: rows[0]], projected[: rows[1]]
        side_in = jnp.concatenate([contract_rows(total[0], p_in), precise_dot(p_in.T, p_in)], axis=0)
        side_out = jnp.concatenate([contract_rows(total[1], p_out), precise_dot(p_out.T, p_out)], axis=0)
        mine = pick(pad_rows(side_in, col_pad), pad_rows(side_out, col_pad))
        column = gather_sum(mine, "shard")
        gram = pick(column[cols[0] : cols[0] + rank], column[cols[1] : cols[1] + rank])
        inverse = inverse_root(gram[None])[0]
        return precise_dot(projected, inverse), precise_dot(column, inverse) / replicas

    part_in = pad_rows(precise_dot(merged[0], inproj_query), row_pad)
    part_out = pad_rows(precise_dot(merged[1], outproj_query), row_pad)
    n = lax.axis_size("replica")
    to_first = (lax.broadcasted_iota(jnp.int32, (n, 1, 1), 0) % 2) == 0
    outgoing = jnp.where(to_first, part_in[None], part_out[None])
    mine = jnp.sum(lax.all_to_all(outgoing, "replica", 0, 0, tiled=False), axis=0)
    projected = gather_sum(mine, "tensor") / replicas
    ortho, query = column_step(projected)
    for _ in range(1, ROUNDS):
        part_in = precise_dot(total[0], query[: cols[0]])
        part_out = precise_dot(total[1], query[: cols[1]])
        mine = pick(pad_rows(part_in, row_pad), pad_rows(part_out, row_pad))
        projected = gather_sum(mine, "tensor") / replicas
        ortho, query = column_step(projected)
    held = jnp.concatenate([ortho, query], axis=0)
    other = lax.ppermute(held, "replica", [(i, i ^ 1) for i in range(n)])
    own_in = pick(held, other)
    own_out = pick(other, held)
    orthos = [own_in[: rows[0]], own_out[: rows[1]]]
    queries = [own_in[row_pad : row_pad + cols[0]], own_out[row_pad : row_pad + cols[1]]]
    first = finish(merged[0], orthos[0], queries[0], inproj_weight, inproj_moment)
    second = finish(merged[1], orthos[1], queries[1], outproj_weight, outproj_moment)
    return (first[0], first[1], first[2], first[3], second[0], second[1], second[2], second[3])


def solution(mesh):
    return jax.shard_map(
        per_device,
        mesh=mesh,
        in_specs=(
            P("replica", "shard", "tensor"),
            P("replica", "shard", "tensor"),
            P("shard", "tensor"),
            P("shard", "tensor"),
            P("tensor", None),
            P("replica", "shard", "tensor"),
            P("replica", "shard", "tensor"),
            P("shard", "tensor"),
            P("shard", "tensor"),
            P("tensor", None),
        ),
        out_specs=(
            P("shard", "tensor"),
            P("shard", "tensor"),
            P("replica", "shard", "tensor"),
            P("tensor", None),
            P("shard", "tensor"),
            P("shard", "tensor"),
            P("replica", "shard", "tensor"),
            P("tensor", None),
        ),
        check_vma=False,
    )
```
